512 devices in a mesh: grp: 16 (over z, core), tok: 32 (over y, x).
Axes of the slice: x: 4, y: 8, z: 8, core: 2. Of those that a mesh axis runs over, the one named last changes fastest.
Arguments:
- patches: bfloat16 [32, 256, 1664], P('tok', 'grp'), may hold values from -54 to 54
- segment_ids: int32 [32, 256], P('tok'), may hold values from 0 to 32, as said below
- padding: int32 [32, 256], P('tok'), may hold values from 0 to 1, as said below
- request_owner: int32 [32, 32], P('tok'), may hold values from 0 to 31, as said below
- first_gain: float32 [1664], replicated, may hold values from 0.5 to 1.5
- first_shift: float32 [1664], replicated, may hold values from -3 to 3
- input_weight: bfloat16 [1664, 16, 312], P(None, 'grp'), may hold values from -0.15625 to 0.15625
- input_shift: float32 [16, 312], P('grp'), may hold values from -40 to 40
- output_weight: bfloat16 [16, 104, 1664], P('grp'), may hold values from -0.15625 to 0.15625
- output_shift: float32 [1664], replicated, may hold values from -3 to 3
- second_gain: float32 [1664], replicated, may hold values from 0.5 to 1.5
- second_shift: float32 [1664], replicated, may hold values from -3 to 3
- up_weight: bfloat16 [1664, 4096], P(None, 'grp'), may hold values from -0.15625 to 0.15625
- up_shift: float32 [4096], P('grp'), may hold values from -3 to 3
- down_weight: bfloat16 [4096, 1664], P('grp'), may hold values from -0.09375 to 0.09375
- down_shift: float32 [1664], replicated, may hold values from -3 to 3
- merge_weight: bfloat16 [6656, 1664], P(None, 'grp'), may hold values from -0.078125 to 0.078125
- merge_shift: float32 [1664], P('grp'), may hold values from -3 to 3
Outputs:
- routed: bfloat16 [32, 32, 8, 1664], P('tok', None, None, 'grp')
The draws below stay inside these ranges and needn't reach their ends.
Inputs may be any that keep to these rules, and one draw needn't show every extreme that they name: `segment_ids`: patches come in aligned runs of four with one id (a 2x2 window); ids never fall along a group; an image spans 1 to 8 windows; every group holds an image of exactly 8 windows; padding stands at the end of a group and carries the id 32. `padding`: 0 exactly where segment_ids is 32. `request_owner`: every row is a permutation of 0 to 31; in every draw one owner receives an image of 8 windows from every group.
All inputs are finite; a program needn't handle non-finite values.
Results may differ from the reference program's by a relative error of at most 0.02.
The reference program's roundings to bfloat16 on the way count: a program that leaves them out, or rounds other values in their place, can miss the bound.
Values may be sent and summed in bfloat16 or wider, within the bound.
No kernel may reach another device: no remote copies, remote signals or barrier semaphores. Data moves between devices by JAX's collectives and lax.ppermute only.
A program may use at most 64 MiB of HBM per device.

```python
import math
import jax
import jax.numpy as jnp
from jax import lax

D = 1664
HEADS = 16
HD = 104
FF_WIN = 4096
CAP = 8
GROUPS = 32
SEQ = 256
SHARDS = 16


def group_layout(key):
    folded = jax.random.fold_in(key, 7)
    key_sizes, key_count, key_live = jax.random.split(folded, 3)
    window_count = SEQ // 4
    column_ids = jnp.arange(GROUPS)[None, :]
    image_sizes = jax.random.randint(key_sizes, (GROUPS, GROUPS), 1, CAP + 1)
    image_sizes = jnp.where(column_ids == 0, CAP, image_sizes)
    used_count = jax.random.randint(key_count, (GROUPS, 1), (GROUPS + 1) // 2, GROUPS + 1)
    image_sizes = jnp.where(column_ids < used_count, image_sizes, 0)
    image_ends = jnp.cumsum(image_sizes, axis=1)
    live_count = jax.random.randint(key_live, (GROUPS, 1), max(CAP, window_count // 2), window_count)
    live_count = jnp.minimum(live_count, image_ends[:, -1:])
    places = jnp.arange(window_count)
    window_live = (places[None, :] < live_count).astype(jnp.int32)
    window_ids = jnp.sum((image_ends[:, None, :] <= places[None, :, None]).astype(jnp.int32), axis=2)
    window_ids = jnp.where(window_live == 1, window_ids, GROUPS)
    return (jnp.repeat(window_ids, 4, axis=1).astype(jnp.int32), jnp.repeat(window_live, 4, axis=1).astype(jnp.int32))


def draw_segment_ids(key, part):
    return group_layout(key)[0]


def draw_padding(key, part):
    return group_layout(key)[1]


def draw_request_owner(key, part):
    folded = jax.random.fold_in(key, 13)
    key_chosen, key_shuffle = jax.random.split(folded)
    chosen = jax.random.randint(key_chosen, (), 0, GROUPS)
    shuffle_keys = jax.random.split(key_shuffle, GROUPS)
    shuffles = jax.vmap(lambda single: jax.random.permutation(single, GROUPS))(shuffle_keys)
    column_ids = jnp.arange(GROUPS)[None, :]
    position = jnp.sum(jnp.where(shuffles == chosen, column_ids, 0), axis=1)
    leading = shuffles[:, :1]
    swapped = jnp.where(column_ids == position[:, None], leading, shuffles)
    return jnp.where(column_ids == 0, chosen, swapped).astype(jnp.int32)


def draw_patches(key, part):
    folded = jax.random.fold_in(key, 3)
    key_base, key_rows, key_cols = jax.random.split(folded, 3)
    row_scale = jnp.exp(jax.random.uniform(key_rows, (GROUPS, SEQ, 1), minval=math.log(0.3), maxval=math.log(3.0)))
    col_scale = jnp.exp(jax.random.uniform(key_cols, (1, 1, D), minval=math.log(0.3), maxval=math.log(3.0)))
    values = jnp.clip(jax.random.normal(key_base, (GROUPS, SEQ, D)), -6.0, 6.0)
    return (values * row_scale * col_scale).astype(jnp.bfloat16)


def draw_input_shift(key, part):
    folded = jax.random.fold_in(key, 5)
    key_one = jax.random.fold_in(folded, 0)
    values = 0.5 * jnp.clip(jax.random.normal(key_one, (HEADS, 3 * HD)), -3.0, 3.0)
    return values.astype(jnp.float32)


def block_scale(stream_key, extent, cuts, low, top_value):
    def one(dim, parts):
        draws = jax.random.uniform(jax.random.fold_in(jax.random.fold_in(stream_key, 6), dim), (parts,), jnp.float32, low / len(cuts), top_value / len(cuts))
        return jnp.repeat(jnp.exp(draws), extent[dim] // parts).reshape((-1,) + (1,) * (len(extent) - dim - 1))

    gain = one(*cuts[0])
    for cut in cuts[1:]:
        gain = gain * one(*cut)
    return gain


def gaussian(rng, dims, scale, reach, cuts=(), kind=jnp.bfloat16):
    drawn = scale * jax.random.normal(rng, dims, jnp.float32)
    if cuts:
        drawn = drawn * block_scale(rng, dims, cuts, -0.22, 0.18)
    return jnp.clip(drawn, -reach, reach).astype(kind)


def setup_inputs(seed: int = 0) -> dict:
    arg_keys = jax.random.split(jax.random.key(seed), 19)
    return {
        "patches": draw_patches(jax.random.fold_in(arg_keys[18], 71), 0),
        "segment_ids": draw_segment_ids(jax.random.fold_in(arg_keys[18], 71), 0),
        "padding": draw_padding(jax.random.fold_in(arg_keys[18], 71), 0),
        "request_owner": draw_request_owner(jax.random.fold_in(arg_keys[18], 71), 0),
        "first_gain": jnp.clip(1.0 + 0.1 * jax.random.normal(arg_keys[4], (D,), jnp.float32), 0.5, 1.5),
        "first_shift": gaussian(arg_keys[5], (D,), 0.5, 3.0, (), jnp.float32),
        "input_weight": gaussian(arg_keys[6], (D, HEADS, 3 * HD), D ** -0.5, 0.15625, ((1, 16),)),
        "input_shift": draw_input_shift(jax.random.fold_in(arg_keys[18], 71), 0),
        "output_weight": gaussian(arg_keys[8], (HEADS, HD, D), D ** -0.5, 0.15625, ((0, 16),)),
        "output_shift": gaussian(arg_keys[9], (D,), 0.5, 3.0, (), jnp.float32),
        "second_gain": jnp.clip(1.0 + 0.1 * jax.random.normal(arg_keys[10], (D,), jnp.float32), 0.5, 1.5),
        "second_shift": gaussian(arg_keys[11], (D,), 0.5, 3.0, (), jnp.float32),
        "up_weight": gaussian(arg_keys[12], (D, FF_WIN), D ** -0.5, 0.15625, ((1, 16),)),
        "up_shift": gaussian(arg_keys[13], (FF_WIN,), 0.5, 3.0, ((0, 16),), jnp.float32),
        "down_weight": gaussian(arg_keys[14], (FF_WIN, D), FF_WIN ** -0.5, 0.09375, ((0, 16),)),
        "down_shift": gaussian(arg_keys[15], (D,), 0.5, 3.0, (), jnp.float32),
        "merge_weight": gaussian(arg_keys[16], (4 * D, D), (4 * D) ** -0.5, 0.078125, ((1, 16),)),
        "merge_shift": gaussian(arg_keys[17], (D,), 0.5, 3.0, ((0, 16),), jnp.float32),
    }


epsilon = 1e-06

def normalize(stream, factor, adjust):
    average = lax.optimization_barrier(jnp.mean(stream, axis=-1, keepdims=True))
    centered = stream - average
    variance = lax.optimization_barrier(jnp.mean(centered * centered, axis=-1, keepdims=True))
    return centered * lax.rsqrt(variance + epsilon) * factor + adjust

def rounded_sum(partials):
    lowered = lax.optimization_barrier(partials.astype(jnp.bfloat16))
    return lax.optimization_barrier(jnp.sum(lowered.astype(jnp.float32), axis=0))

def attention_mask(segments, live_rows):
    count = segments.shape[0]
    same_image = segments[:, None] == segments[None, :]
    allowed = jnp.logical_and(same_image, live_rows[None, :] == 1)
    diagonal = jnp.arange(count)[:, None] == jnp.arange(count)[None, :]
    return jnp.logical_or(allowed, diagonal)

def softmax_rows(scores, allowed):
    masked = jnp.where(allowed, scores, -jnp.inf)
    row_max = lax.optimization_barrier(jnp.max(masked, axis=-1, keepdims=True))
    powered = jnp.where(allowed, jnp.exp(masked - row_max), 0.0)
    return powered / lax.optimization_barrier(jnp.sum(powered, axis=-1, keepdims=True))

def routed_rows(merged, segments, live_rows, owners):
    window_segments = segments[::4]
    window_live = live_rows[::4]
    window_count = window_segments.shape[0]
    places = jnp.arange(window_count)
    earlier = jnp.logical_and(window_segments[None, :] == window_segments[:, None], places[None, :] < places[:, None])
    slot_index = lax.optimization_barrier(jnp.sum(earlier.astype(jnp.int32), axis=1))
    groups = owners.shape[0]
    matched = (jnp.arange(groups)[None, :] == window_segments[:, None]).astype(jnp.int32)
    owner_of = lax.optimization_barrier(jnp.sum(matched * owners[None, :], axis=1))
    target = owner_of * CAP + slot_index
    one_hot = jnp.logical_and(target[:, None] == jnp.arange(groups * CAP)[None, :], window_live[:, None] == 1)
    outgoing = jnp.einsum('wc,wd->cd', one_hot.astype(jnp.float32), merged.astype(jnp.float32))
    return outgoing.astype(jnp.bfloat16).reshape(groups, CAP, merged.shape[1])

def reference(patches, segment_ids, padding, request_owner, first_gain, first_shift, input_weight, input_shift, output_weight, output_shift, second_gain, second_shift, up_weight, up_shift, down_weight, down_shift, merge_weight, merge_shift):
    heads_set = HEADS // SHARDS
    units_set = FF_WIN // SHARDS

    def one_group(group_index):
        stream = patches[group_index].astype(jnp.float32)
        segments = segment_ids[group_index]
        live_rows = padding[group_index]
        normed = normalize(stream, first_gain, first_shift).astype(jnp.bfloat16)
        projected = jnp.einsum('sd,dhe->hse', normed.astype(jnp.float32), input_weight.astype(jnp.float32))
        projected = (projected + input_shift[:, None, :]).astype(jnp.bfloat16)
        queries = projected[:, :, :HD].astype(jnp.float32)
        key_rows = projected[:, :, HD:2 * HD].astype(jnp.float32)
        value_rows = projected[:, :, 2 * HD:].astype(jnp.float32)
        scores = jnp.einsum('hqe,hke->hqk', queries, key_rows) * HD ** (-0.5)
        probabilities = softmax_rows(scores, attention_mask(segments, live_rows)[None]).astype(jnp.bfloat16)
        mixed = jnp.einsum('hqk,hke->hqe', probabilities.astype(jnp.float32), value_rows).astype(jnp.bfloat16)
        partials = jnp.einsum('jhqe,jhed->jqd', mixed.reshape(SHARDS, heads_set, SEQ, HD).astype(jnp.float32), output_weight.reshape(SHARDS, heads_set, HD, D).astype(jnp.float32))
        residual = (stream + rounded_sum(partials) + output_shift).astype(jnp.bfloat16)
        normed_again = normalize(residual.astype(jnp.float32), second_gain, second_shift).astype(jnp.bfloat16)
        lifted = jnp.dot(normed_again, up_weight, preferred_element_type=jnp.float32) + up_shift
        activated = jax.nn.gelu(lifted, approximate=False).astype(jnp.bfloat16)
        partials_two = jnp.einsum('sjf,jfd->jsd', activated.reshape(SEQ, SHARDS, units_set).astype(jnp.float32), down_weight.reshape(SHARDS, units_set, D).astype(jnp.float32))
        layer_out = (residual.astype(jnp.float32) + rounded_sum(partials_two) + down_shift).astype(jnp.bfloat16)
        windows = layer_out.reshape(SEQ // 4, 4 * D)
        merged = (jnp.dot(windows, merge_weight, preferred_element_type=jnp.float32) + merge_shift).astype(jnp.bfloat16)
        return routed_rows(merged, segments, live_rows, request_owner[group_index])
    outgoing = lax.map(one_group, jnp.arange(GROUPS))
    return jnp.transpose(outgoing, (1, 0, 2, 3))
```

```python
import jax
import jax.numpy as jnp
from jax import lax
from jax.sharding import PartitionSpec as P

CAP = 8


epsilon = 1e-06


def normalize(stream, factor, adjust):
    average = jnp.mean(stream, axis=-1, keepdims=True)
    centered = stream - average
    variance = jnp.mean(centered * centered, axis=-1, keepdims=True)
    return centered * lax.rsqrt(variance + epsilon) * factor + adjust


def attention_mask(segments, live_rows):
    count = segments.shape[0]
    same_image = segments[:, None] == segments[None, :]
    allowed = jnp.logical_and(same_image, live_rows[None, :] == 1)
    diagonal = jnp.arange(count)[:, None] == jnp.arange(count)[None, :]
    return jnp.logical_or(allowed, diagonal)


def softmax_rows(scores, allowed):
    masked = jnp.where(allowed, scores, -jnp.inf)
    row_max = jnp.max(masked, axis=-1, keepdims=True)
    powered = jnp.where(allowed, jnp.exp(masked - row_max), 0.0)
    return powered / jnp.sum(powered, axis=-1, keepdims=True)


def attend(projected, segments, live_rows, head_dim):
    queries = projected[:, :, :head_dim]
    key_rows = projected[:, :, head_dim : 2 * head_dim]
    value_rows = projected[:, :, 2 * head_dim :]
    scores = jnp.einsum(
        "qhe,khe->hqk", queries, key_rows, preferred_element_type=jnp.float32
    ) * head_dim ** (-0.5)
    probabilities = softmax_rows(scores, attention_mask(segments, live_rows)[None]).astype(
        jnp.bfloat16
    )
    return jnp.einsum(
        "hqk,khe->qhe", probabilities, value_rows, preferred_element_type=jnp.float32
    ).astype(jnp.bfloat16)


def summed_apart(terms):
    shards = lax.psum(1, "grp")
    rows = terms.shape[0] // shards
    pieces = lax.all_to_all(
        terms.reshape(shards, rows, terms.shape[1]), "grp", 0, 0, tiled=False
    )
    return jnp.sum(pieces.astype(jnp.float32), axis=0)


def routed_rows(merged, segments, live_rows, owners):
    window_segments = segments[::4]
    window_live = live_rows[::4]
    window_count = window_segments.shape[0]
    places = jnp.arange(window_count)
    earlier = jnp.logical_and(
        window_segments[None, :] == window_segments[:, None], places[None, :] < places[:, None]
    )
    slot_index = jnp.sum(earlier.astype(jnp.int32), axis=1)
    groups = owners.shape[0]
    matched = (jnp.arange(groups)[None, :] == window_segments[:, None]).astype(jnp.int32)
    owner_of = jnp.sum(matched * owners[None, :], axis=1)
    target = owner_of * CAP + slot_index
    one_hot = jnp.logical_and(
        target[:, None] == jnp.arange(groups * CAP)[None, :], window_live[:, None] == 1
    )
    outgoing = jnp.einsum(
        "wc,wd->cd", one_hot.astype(jnp.bfloat16), merged, preferred_element_type=jnp.float32
    )
    return outgoing.astype(jnp.bfloat16).reshape(groups, CAP, merged.shape[1])


def on_device(
    patches,
    segment_ids,
    padding,
    request_owner,
    first_gain,
    first_shift,
    input_weight,
    input_shift,
    output_weight,
    output_shift,
    second_gain,
    second_shift,
    up_weight,
    up_shift,
    down_weight,
    down_shift,
    merge_weight,
    merge_shift,
):
    row_count = patches.shape[1]
    model_width = patches.shape[2]
    head_dim = input_weight.shape[2] // 3
    segments = segment_ids[0]
    live_rows = padding[0]
    stream = patches[0]
    normed = normalize(stream.astype(jnp.float32), first_gain, first_shift).astype(jnp.bfloat16)
    lifted = jnp.einsum(
        "sd,dhe->she",
        lax.all_gather(normed, "grp", axis=0, tiled=True),
        input_weight,
        preferred_element_type=jnp.float32,
    )
    projected = (lifted + input_shift[None]).astype(jnp.bfloat16)
    mixed = attend(projected, segments, live_rows, head_dim)
    block = mixed
    attended = summed_apart(
        jnp.einsum("qhe,hed->qd", block, output_weight, preferred_element_type=jnp.float32).astype(
            jnp.bfloat16
        )
    )
    residual = (stream.astype(jnp.float32) + attended + output_shift).astype(jnp.bfloat16)
    normed_again = normalize(residual.astype(jnp.float32), second_gain, second_shift).astype(
        jnp.bfloat16
    )
    lifted = (
        jnp.dot(
            lax.all_gather(normed_again, "grp", axis=0, tiled=True),
            up_weight,
            preferred_element_type=jnp.float32,
        )
        + up_shift
    )
    activated = jax.nn.gelu(lifted, approximate=False).astype(jnp.bfloat16)
    block = activated
    fed = summed_apart(
        jnp.dot(block, down_weight, preferred_element_type=jnp.float32).astype(jnp.bfloat16)
    )
    layer_out = (residual.astype(jnp.float32) + fed + down_shift).astype(jnp.bfloat16)
    windows = layer_out.reshape(row_count // 4, 4 * model_width)
    merged = (
        jnp.dot(
            lax.all_gather(windows, "grp", axis=0, tiled=True),
            merge_weight,
            preferred_element_type=jnp.float32,
        )
        + merge_shift
    ).astype(jnp.bfloat16)
    outgoing = routed_rows(merged, segments, live_rows, request_owner[0])
    delivered = lax.all_to_all(outgoing, "tok", split_axis=0, concat_axis=0, tiled=True)
    return delivered[None]


def solution(mesh):
    return jax.shard_map(
        on_device,
        mesh=mesh,
        in_specs=(
            P("tok", "grp", None),
            P("tok", None),
            P("tok", None),
            P("tok", None),
            P(),
            P(),
            P(None, "grp", None),
            P("grp", None),
            P("grp", None, None),
            P(),
            P(),
            P(),
            P(None, "grp"),
            P("grp"),
            P("grp", None),
            P(),
            P(None, "grp"),
            P("grp"),
        ),
        out_specs=P("tok", None, None, "grp"),
        check_vma=False,
    )
```

```python
import jax
import jax.numpy as jnp
from jax import lax
from jax.sharding import PartitionSpec as P

CAP = 8


epsilon = 1e-06


def normalize(stream, factor, adjust):
    average = jnp.mean(stream, axis=-1, keepdims=True)
    centered = stream - average
    variance = jnp.mean(centered * centered, axis=-1, keepdims=True)
    return centered * lax.rsqrt(variance + epsilon) * factor + adjust


def attention_mask(segments, live_rows):
    count = segments.shape[0]
    same_image = segments[:, None] == segments[None, :]
    allowed = jnp.logical_and(same_image, live_rows[None, :] == 1)
    diagonal = jnp.arange(count)[:, None] == jnp.arange(count)[None, :]
    return jnp.logical_or(allowed, diagonal)


def softmax_rows(scores, allowed):
    masked = jnp.where(allowed, scores, -jnp.inf)
    row_max = jnp.max(masked, axis=-1, keepdims=True)
    powered = jnp.where(allowed, jnp.exp(masked - row_max), 0.0)
    return powered / jnp.sum(powered, axis=-1, keepdims=True)


def attend(projected, segments, live_rows, head_dim):
    queries = projected[:, :, :head_dim]
    key_rows = projected[:, :, head_dim : 2 * head_dim]
    value_rows = projected[:, :, 2 * head_dim :]
    scores = jnp.einsum(
        "qhe,khe->hqk", queries, key_rows, preferred_element_type=jnp.float32
    ) * head_dim ** (-0.5)
    probabilities = lax.optimization_barrier(
        softmax_rows(scores, attention_mask(segments, live_rows)[None]).astype(jnp.bfloat16)
    )
    return jnp.einsum(
        "hqk,khe->qhe", probabilities, value_rows, preferred_element_type=jnp.float32
    ).astype(jnp.bfloat16)


def summed_apart(terms):
    shards = lax.psum(1, "grp")
    rows = terms.shape[0] // shards
    pieces = lax.all_to_all(
        terms.reshape(shards, rows, terms.shape[1]), "grp", 0, 0, tiled=False
    )
    return jnp.sum(pieces.astype(jnp.float32), axis=0)


def routed_rows(merged, segments, live_rows, owners):
    window_segments = segments[::4]
    window_live = live_rows[::4]
    window_count = window_segments.shape[0]
    places = jnp.arange(window_count)
    earlier = jnp.logical_and(
        window_segments[None, :] == window_segments[:, None], places[None, :] < places[:, None]
    )
    slot_index = jnp.sum(earlier.astype(jnp.int32), axis=1)
    groups = owners.shape[0]
    matched = (jnp.arange(groups)[None, :] == window_segments[:, None]).astype(jnp.int32)
    owner_of = jnp.sum(matched * owners[None, :], axis=1)
    target = owner_of * CAP + slot_index
    one_hot = jnp.logical_and(
        target[:, None] == jnp.arange(groups * CAP)[None, :], window_live[:, None] == 1
    )
    outgoing = jnp.einsum(
        "wc,wd->cd", one_hot.astype(jnp.bfloat16), merged, preferred_element_type=jnp.float32
    )
    return outgoing.astype(jnp.bfloat16).reshape(groups, CAP, merged.shape[1])


def on_device(
    patches,
    segment_ids,
    padding,
    request_owner,
    first_gain,
    first_shift,
    input_weight,
    input_shift,
    output_weight,
    output_shift,
    second_gain,
    second_shift,
    up_weight,
    up_shift,
    down_weight,
    down_shift,
    merge_weight,
    merge_shift,
):
    row_count = patches.shape[1]
    model_width = patches.shape[2]
    head_dim = input_weight.shape[2] // 3
    segments = segment_ids[0]
    live_rows = padding[0]
    stream = patches[0]
    gathered = lax.all_gather(stream, "grp", axis=0, tiled=True)
    normed = normalize(gathered.astype(jnp.float32), first_gain, first_shift).astype(jnp.bfloat16)
    lifted = jnp.einsum(
        "sd,dhe->she",
        normed,
        input_weight,
        preferred_element_type=jnp.float32,
    )
    projected = (lifted + input_shift[None]).astype(jnp.bfloat16)
    mixed = attend(projected, segments, live_rows, head_dim)
    block = lax.optimization_barrier(mixed)
    attended = summed_apart(
        jnp.einsum("qhe,hed->qd", block, output_weight, preferred_element_type=jnp.float32).astype(
            jnp.bfloat16
        )
    )
    residual = (stream.astype(jnp.float32) + attended + output_shift).astype(jnp.bfloat16)
    normed_again = normalize(residual.astype(jnp.float32), second_gain, second_shift).astype(
        jnp.bfloat16
    )
    lifted = (
        jnp.dot(
            lax.all_gather(normed_again, "grp", axis=0, tiled=True),
            up_weight,
            preferred_element_type=jnp.float32,
        )
        + up_shift
    )
    activated = jax.nn.gelu(lifted, approximate=False).astype(jnp.bfloat16)
    block = lax.optimization_barrier(activated)
    fed = summed_apart(
        jnp.dot(block, down_weight, preferred_element_type=jnp.float32).astype(jnp.bfloat16)
    )
    layer_out = (residual.astype(jnp.float32) + fed + down_shift).astype(jnp.bfloat16)
    windows = layer_out.reshape(row_count // 4, 4 * model_width)
    merged = (
        jnp.dot(
            lax.all_gather(windows, "grp", axis=0, tiled=True),
            merge_weight,
            preferred_element_type=jnp.float32,
        )
        + merge_shift
    ).astype(jnp.bfloat16)
    outgoing = routed_rows(merged, segments, live_rows, request_owner[0])
    delivered = lax.all_to_all(outgoing, "tok", split_axis=0, concat_axis=0, tiled=True)
    return delivered[None]


def solution(mesh):
    return jax.shard_map(
        on_device,
        mesh=mesh,
        in_specs=(
            P("tok", "grp", None),
            P("tok", None),
            P("tok", None),
            P("tok", None),
            P(),
            P(),
            P(None, "grp", None),
            P("grp", None),
            P("grp", None, None),
            P(),
            P(),
            P(),
            P(None, "grp"),
            P("grp"),
            P("grp", None),
            P(),
            P(None, "grp"),
            P("grp"),
        ),
        out_specs=P("tok", None, None, "grp"),
        check_vma=False,
    )
```
